1024 devices in a mesh: rows: 64 (over z, core), dp: 16 (over x, y).
Axes of the slice: x: 4, y: 4, z: 32, core: 2. Of those that a mesh axis runs over, the one named last changes fastest.
Arguments:
- features: bfloat16 [48, 3456, 2048], P('dp', 'rows'), may hold values from -6 to 6
- depth_weight: bfloat16 [9, 2048], P(None, 'rows'), may hold values from -2 to 2
- point_weight: bfloat16 [2048, 256], replicated, may hold values from -0.125 to 0.125
- cotangent: bfloat16 [48, 3456, 256], P('dp', 'rows'), may hold values from -6 to 6
Outputs:
- branch_out: bfloat16 [48, 3456, 256], P('dp', 'rows')
- grad_features: bfloat16 [48, 3456, 2048], P('dp', None, 'rows')
- grad_point: float32 [2048, 256], P('rows')
- grad_depth: float32 [9, 2048], P(None, 'rows')
The draws below stay inside these ranges and needn't reach their ends.
All inputs are finite; a program needn't handle non-finite values.
Results may differ from the reference program's by a relative error of at most 0.0061.
Values may be sent and summed in bfloat16 or wider, within the bound.
No kernel may reach another device: no remote copies, remote signals or barrier semaphores. Data moves between devices by JAX's collectives and lax.ppermute only.
A program may use at most 32 MiB of HBM per device.

```python
import math
import jax
import jax.numpy as jnp
from jax import lax

C = 2048
K = 256
DILATION_STEP = 12
H16 = 48
W16 = 72
B = 48
PIX = 3456


def steps_of(key, dims, cuts, low, high):
    factor_of = 1.0
    for position, parts in cuts:
        draws = jax.random.uniform(jax.random.fold_in(jax.random.fold_in(key, 6), position), (parts,), jnp.float32, low / len(cuts), high / len(cuts))
        factor_of = factor_of * jnp.repeat(jnp.exp(draws), dims[position] // parts).reshape((-1,) + (1,) * (len(dims) - 1 - position))
    return factor_of


def bell_draw(rng, shape, spread, reach, pieces=(), dtype=jnp.bfloat16):
    entries = spread * jax.random.normal(rng, shape, jnp.float32)
    if pieces:
        entries = entries * steps_of(rng, shape, pieces, -0.22, 0.18)
    return jnp.clip(entries, -reach, reach).astype(dtype)


def setup_inputs(seed: int = 0) -> dict:
    key_of = jax.random.split(jax.random.key(seed), 5)
    features = bell_draw(key_of[0], (B, PIX, C), 1.0, 6.0, ((0, 16), (1, 64)))
    depth_weight = bell_draw(key_of[1], (9, C), 9 ** -0.5, 2.0, ((1, 64),))
    point_weight = bell_draw(key_of[2], (C, K), C ** -0.5, 0.125)
    cotangent = bell_draw(key_of[3], (B, PIX, K), 1.0, 6.0, ((0, 16), (1, 64)))
    return dict(features=features, depth_weight=depth_weight, point_weight=point_weight, cotangent=cotangent)


def gelu_tanh(value):
    return jax.nn.gelu(value, approximate=True)

def tap_view(padded_grid, row_offset, column_offset, height, width):
    top_border = DILATION_STEP + DILATION_STEP * row_offset
    left_border = DILATION_STEP + DILATION_STEP * column_offset
    return padded_grid[top_border:top_border + height, left_border:left_border + width, :]

def depthwise(feature_grid, kernel, sign):
    height, width = (feature_grid.shape[0], feature_grid.shape[1])
    padded_grid = jnp.pad(feature_grid, ((DILATION_STEP, DILATION_STEP), (DILATION_STEP, DILATION_STEP), (0, 0))).astype(jnp.float32)
    total = jnp.zeros(feature_grid.shape, jnp.float32)
    for row_offset in range(-1, 2):
        for column_offset in range(-1, 2):
            index = 3 * (row_offset + 1) + (column_offset + 1)
            view = tap_view(padded_grid, sign * row_offset, sign * column_offset, height, width)
            total = total + view * kernel[index].astype(jnp.float32)
    return total

def tap_sums(grad_mixed, feature_grid):
    height, width = (feature_grid.shape[0], feature_grid.shape[1])
    padded_grid = jnp.pad(feature_grid, ((DILATION_STEP, DILATION_STEP), (DILATION_STEP, DILATION_STEP), (0, 0))).astype(jnp.float32)
    upstream = grad_mixed.astype(jnp.float32)
    rows_out = []
    for row_offset in range(-1, 2):
        for column_offset in range(-1, 2):
            view = tap_view(padded_grid, row_offset, column_offset, height, width)
            rows_out.append(lax.optimization_barrier(jnp.sum(upstream * view, axis=(0, 1))))
    return jnp.stack(rows_out, axis=0)

def reference(features, depth_weight, point_weight, cotangent):
    chans = features.shape[2]

    def one_sample(carry, inputs):
        flat_field, upstream = inputs
        feature_grid = flat_field.reshape(H16, W16, chans)
        mixed = depthwise(feature_grid, depth_weight, 1).astype(jnp.bfloat16)
        flat = mixed.reshape(-1, chans)
        pre = jnp.dot(flat, point_weight, preferred_element_type=jnp.float32)
        act, pull = jax.vjp(gelu_tanh, pre)
        grad_pre = pull(upstream.astype(jnp.float32))[0].astype(jnp.bfloat16)
        grad_mixed = lax.dot_general(grad_pre, point_weight, (((1,), (1,)), ((), ())), preferred_element_type=jnp.float32)
        grad_mixed = grad_mixed.astype(jnp.bfloat16).reshape(H16, W16, chans)
        point_part = lax.dot_general(flat, grad_pre, (((0,), (0,)), ((), ())), preferred_element_type=jnp.float32)
        grad_field = depthwise(grad_mixed, depth_weight, -1).astype(jnp.bfloat16).reshape(-1, chans)
        depth_part = tap_sums(grad_mixed, feature_grid)
        carry = (carry[0] + point_part, carry[1] + depth_part)
        return (carry, (act.astype(jnp.bfloat16), grad_field))
    start = (jnp.zeros((chans, K), jnp.float32), jnp.zeros((9, chans), jnp.float32))
    sums, outputs = lax.scan(one_sample, start, (features, cotangent))
    scale = 1.0 / math.sqrt(features.shape[0] * H16 * W16)
    return (outputs[0], outputs[1], sums[0] * scale, sums[1] * scale)
```

```python
import math

import jax
import jax.numpy as jnp
from jax import lax
from jax.sharding import PartitionSpec as P

K = 256
DILATION_STEP = 12
H16 = 48
W16 = 72


def gelu_tanh(value):
    return jax.nn.gelu(value, approximate=True)


def padded_flat(flat_grid):
    reach = DILATION_STEP * W16 + DILATION_STEP
    return jnp.pad(flat_grid, ((0, 0), (0, 0), (reach, reach)))


def shifted(padded_grid, pixels, row_offset, column_offset):
    reach = DILATION_STEP * W16 + DILATION_STEP
    start = reach + DILATION_STEP * (row_offset * W16 + column_offset)
    view = padded_grid[:, :, start : start + pixels].astype(jnp.float32)
    column = jnp.arange(pixels, dtype=jnp.int32) % W16 + DILATION_STEP * column_offset
    keep = jnp.logical_and(column >= 0, column < W16)
    return jnp.where(keep, view, 0.0)


def depthwise(flat_grid, kernel, sign):
    pixels = flat_grid.shape[2]
    padded_grid = padded_flat(flat_grid)
    total = jnp.zeros(flat_grid.shape, jnp.float32)
    for row_offset in range(-1, 2):
        for column_offset in range(-1, 2):
            index = 3 * (row_offset + 1) + (column_offset + 1)
            view = shifted(padded_grid, pixels, sign * row_offset, sign * column_offset)
            total = total + view * kernel[index].astype(jnp.float32)[:, None]
    return total


def tap_sums(grad_mixed, flat_grid):
    pixels = flat_grid.shape[2]
    padded_grid = padded_flat(flat_grid)
    upstream = grad_mixed.astype(jnp.float32)
    rows_out = []
    for row_offset in range(-1, 2):
        for column_offset in range(-1, 2):
            view = shifted(padded_grid, pixels, row_offset, column_offset)
            rows_out.append(jnp.sum(upstream * view, axis=(0, 2)))
    return jnp.stack(rows_out, axis=0)


def on_device(features, depth_weight, point_weight, cotangent):
    local_chan = jnp.transpose(features, (0, 2, 1))
    chan_field = lax.all_to_all(local_chan, "rows", split_axis=1, concat_axis=2, tiled=True)
    samples, slice_width, pixels = chan_field.shape
    chan_mixed = depthwise(chan_field, depth_weight, 1).astype(jnp.bfloat16)
    row_mixed = lax.all_to_all(chan_mixed, "rows", split_axis=2, concat_axis=1, tiled=True)
    chans = row_mixed.shape[1]
    here = row_mixed.shape[2]
    flat = jnp.transpose(row_mixed, (0, 2, 1)).reshape(-1, chans)
    pre = jnp.dot(flat, point_weight, preferred_element_type=jnp.float32)
    act, pull = jax.vjp(gelu_tanh, pre)
    branch_out = act.astype(jnp.bfloat16).reshape(samples, here, K)
    grad_pre = pull(cotangent.reshape(-1, K).astype(jnp.float32))[0].astype(jnp.bfloat16)
    grad_pre_all = lax.all_gather(grad_pre.reshape(samples, here, K), "rows", axis=1, tiled=True)
    start = lax.axis_index("rows") * slice_width
    weight_own = lax.dynamic_slice_in_dim(point_weight, start, slice_width, axis=0)
    grad_chan = lax.dot_general(
        weight_own, grad_pre_all, (((1,), (2,)), ((), ())), preferred_element_type=jnp.float32
    )
    grad_chan = jnp.transpose(grad_chan, (1, 0, 2)).astype(jnp.bfloat16)
    point_slice = lax.dot_general(
        chan_mixed, grad_pre_all, (((0, 2), (0, 1)), ((), ())), preferred_element_type=jnp.float32
    )
    grad_field = depthwise(grad_chan, depth_weight, -1).astype(jnp.bfloat16)
    grad_features = jnp.transpose(grad_field, (0, 2, 1))
    depth_part = tap_sums(grad_chan, chan_field)
    grad_point, grad_depth = lax.psum((point_slice, depth_part), "dp")
    scale = 1.0 / math.sqrt(samples * lax.axis_size("dp") * H16 * W16)
    return (branch_out, grad_features, grad_point * scale, grad_depth * scale)


def solution(mesh):
    placed = (P("dp", "rows", None), P(None, "rows"), P(), P("dp", "rows", None))
    return jax.shard_map(
        on_device,
        mesh=mesh,
        in_specs=placed,
        out_specs=(P("dp", "rows", None), P("dp", None, "rows"), P("rows", None), P(None, "rows")),
        check_vma=False,
    )
```

```python
import math

import jax
import jax.numpy as jnp
from jax import lax
from jax.sharding import PartitionSpec as P

K = 256
DILATION_STEP = 12
H16 = 48
W16 = 72


def gelu_tanh(value):
    return jax.nn.gelu(value, approximate=True)


def padded_flat(flat_grid):
    reach = DILATION_STEP * W16 + DILATION_STEP
    return jnp.pad(flat_grid, ((0, 0), (0, 0), (reach, reach)))


def shifted(padded_grid, pixels, row_offset, column_offset):
    reach = DILATION_STEP * W16 + DILATION_STEP
    start = reach + DILATION_STEP * (row_offset * W16 + column_offset)
    view = padded_grid[:, :, start : start + pixels].astype(jnp.float32)
    column = jnp.arange(pixels, dtype=jnp.int32) % W16 + DILATION_STEP * column_offset
    keep = jnp.logical_and(column >= 0, column < W16)
    return jnp.where(keep, view, 0.0)


def depthwise(flat_grid, kernel, sign):
    pixels = flat_grid.shape[2]
    padded_grid = padded_flat(flat_grid)
    total = jnp.zeros(flat_grid.shape, jnp.float32)
    for row_offset in range(-1, 2):
        for column_offset in range(-1, 2):
            index = 3 * (row_offset + 1) + (column_offset + 1)
            view = shifted(padded_grid, pixels, sign * row_offset, sign * column_offset)
            total = total + view * kernel[index].astype(jnp.float32)[:, None]
    return total


def tap_sums(grad_mixed, flat_grid):
    pixels = flat_grid.shape[2]
    padded_grid = padded_flat(flat_grid)
    upstream = grad_mixed.astype(jnp.float32)
    rows_out = []
    for row_offset in range(-1, 2):
        for column_offset in range(-1, 2):
            view = shifted(padded_grid, pixels, row_offset, column_offset)
            rows_out.append(jnp.sum(upstream * view, axis=(0, 2)))
    return jnp.stack(rows_out, axis=0)


def on_device(features, depth_weight, point_weight, cotangent):
    local_chan = jnp.transpose(features, (0, 2, 1))
    chan_field = lax.all_to_all(local_chan, "rows", split_axis=1, concat_axis=2, tiled=True)
    samples, slice_width, pixels = chan_field.shape
    chan_mixed = depthwise(chan_field, depth_weight, 1).astype(jnp.bfloat16)
    row_mixed = lax.all_to_all(chan_mixed, "rows", split_axis=2, concat_axis=1, tiled=True)
    chans = row_mixed.shape[1]
    here = row_mixed.shape[2]
    flat = jnp.transpose(row_mixed, (0, 2, 1)).reshape(-1, chans)
    pre = jnp.dot(flat, point_weight, preferred_element_type=jnp.float32)
    act, pull = jax.vjp(gelu_tanh, pre)
    branch_out = act.astype(jnp.bfloat16).reshape(samples, here, K)
    grad_pre = pull(cotangent.reshape(-1, K).astype(jnp.float32))[0].astype(jnp.bfloat16)
    grad_pre_all = lax.all_gather(grad_pre.reshape(samples, here, K), "rows", axis=1, tiled=True)
    start = lax.axis_index("rows") * slice_width
    weight_own = lax.dynamic_slice_in_dim(point_weight, start, slice_width, axis=0)
    grad_chan = lax.dot_general(
        weight_own, grad_pre_all, (((1,), (2,)), ((), ())), preferred_element_type=jnp.float32
    )
    grad_chan = jnp.transpose(grad_chan, (1, 0, 2)).astype(jnp.bfloat16)
    point_slice = lax.dot_general(
        chan_mixed, grad_pre_all, (((0, 2), (0, 1)), ((), ())), preferred_element_type=jnp.float32
    )
    grad_field = depthwise(grad_chan, depth_weight, -1).astype(jnp.bfloat16)
    grad_features = jnp.transpose(grad_field, (0, 2, 1))
    depth_part = tap_sums(grad_chan, chan_field)
    taps = depth_part.shape[0]
    packed = jnp.concatenate(
        [point_slice, jnp.pad(depth_part, ((0, 0), (0, K - depth_part.shape[1])))], axis=0
    )
    summed = lax.all_gather(packed, "dp", axis=0, tiled=False).sum(axis=0)
    grad_point = summed[:slice_width]
    grad_depth = summed[slice_width : slice_width + taps, : depth_part.shape[1]]
    scale = 1.0 / math.sqrt(samples * lax.axis_size("dp") * H16 * W16)
    return (branch_out, grad_features, grad_point * scale, grad_depth * scale)


def solution(mesh):
    placed = (P("dp", "rows", None), P(None, "rows"), P(), P("dp", "rows", None))
    return jax.shard_map(
        on_device,
        mesh=mesh,
        in_specs=placed,
        out_specs=(P("dp", "rows", None), P("dp", None, "rows"), P("rows", None), P(None, "rows")),
        check_vma=False,
    )
```

```python
import math

import jax
import jax.numpy as jnp
from jax import lax
from jax.sharding import PartitionSpec as P

K = 256
DILATION_STEP = 12
H16 = 48
W16 = 72


def gelu_tanh(value):
    return jax.nn.gelu(value, approximate=True)


def padded_flat(flat_grid):
    reach = DILATION_STEP * W16 + DILATION_STEP
    return jnp.pad(flat_grid, ((0, 0), (reach, reach), (0, 0)))


def shifted(padded_grid, pixels, row_offset, column_offset):
    reach = DILATION_STEP * W16 + DILATION_STEP
    start = reach + DILATION_STEP * (row_offset * W16 + column_offset)
    view = padded_grid[:, start : start + pixels, :].astype(jnp.float32)
    column = jnp.arange(pixels, dtype=jnp.int32) % W16 + DILATION_STEP * column_offset
    keep = jnp.logical_and(column >= 0, column < W16)[:, None]
    return jnp.where(keep, view, 0.0)


def depthwise(flat_grid, kernel, sign):
    pixels = flat_grid.shape[1]
    padded_grid = padded_flat(flat_grid)
    total = jnp.zeros(flat_grid.shape, jnp.float32)
    for row_offset in range(-1, 2):
        for column_offset in range(-1, 2):
            index = 3 * (row_offset + 1) + (column_offset + 1)
            view = shifted(padded_grid, pixels, sign * row_offset, sign * column_offset)
            total = total + view * kernel[index].astype(jnp.float32)
    return total


def tap_sums(grad_mixed, flat_grid):
    pixels = flat_grid.shape[1]
    padded_grid = padded_flat(flat_grid)
    upstream = grad_mixed.astype(jnp.float32)
    rows_out = []
    for row_offset in range(-1, 2):
        for column_offset in range(-1, 2):
            view = shifted(padded_grid, pixels, row_offset, column_offset)
            rows_out.append(jnp.sum(upstream * view, axis=(0, 1)))
    return jnp.stack(rows_out, axis=0)


def on_device(features, depth_weight, point_weight, cotangent):
    samples, here, chans = features.shape
    parts = lax.axis_size("rows")
    slice_width = chans // parts
    blocks = jnp.transpose(features.reshape(samples, here, parts, slice_width), (2, 0, 1, 3))
    arrived = lax.all_to_all(blocks, "rows", split_axis=0, concat_axis=0, tiled=True)
    chan_field = jnp.transpose(arrived, (1, 0, 2, 3)).reshape(samples, parts * here, slice_width)
    chan_mixed = depthwise(chan_field, depth_weight, 1).astype(jnp.bfloat16)
    outgoing = jnp.transpose(chan_mixed.reshape(samples, parts, here, slice_width), (1, 0, 2, 3))
    returned = lax.all_to_all(outgoing, "rows", split_axis=0, concat_axis=0, tiled=True)
    row_mixed = jnp.transpose(returned, (1, 2, 0, 3)).reshape(samples * here, chans)
    pre = jnp.dot(row_mixed, point_weight, preferred_element_type=jnp.float32)
    act, pull = jax.vjp(gelu_tanh, pre)
    branch_out = act.astype(jnp.bfloat16).reshape(samples, here, K)
    grad_pre = pull(cotangent.reshape(-1, K).astype(jnp.float32))[0].astype(jnp.bfloat16)
    grad_pre_all = lax.all_gather(grad_pre.reshape(samples, here, K), "rows", axis=1, tiled=True)
    start = lax.axis_index("rows") * slice_width
    weight_own = lax.dynamic_slice_in_dim(point_weight, start, slice_width, axis=0)
    grad_chan = lax.dot_general(
        grad_pre_all, weight_own, (((2,), (1,)), ((), ())), preferred_element_type=jnp.float32
    ).astype(jnp.bfloat16)
    point_slice = lax.dot_general(
        chan_mixed, grad_pre_all, (((0, 1), (0, 1)), ((), ())), preferred_element_type=jnp.float32
    )
    grad_features = depthwise(grad_chan, depth_weight, -1).astype(jnp.bfloat16)
    depth_part = tap_sums(grad_chan, chan_field)
    taps = depth_part.shape[0]
    packed = jnp.concatenate(
        [point_slice, jnp.pad(depth_part, ((0, 0), (0, K - depth_part.shape[1])))], axis=0
    )
    summed = lax.all_gather(packed, "dp", axis=0, tiled=False).sum(axis=0)
    grad_point = summed[:slice_width]
    grad_depth = summed[slice_width : slice_width + taps, : depth_part.shape[1]]
    scale = 1.0 / math.sqrt(samples * lax.axis_size("dp") * H16 * W16)
    return (branch_out, grad_features, grad_point * scale, grad_depth * scale)


def solution(mesh):
    placed = (P("dp", "rows", None), P(None, "rows"), P(), P("dp", "rows", None))
    return jax.shard_map(
        on_device,
        mesh=mesh,
        in_specs=placed,
        out_specs=(P("dp", "rows", None), P("dp", None, "rows"), P("rows", None), P(None, "rows")),
        check_vma=False,
    )
```

```python
import math

import jax
import jax.numpy as jnp
from jax import lax
from jax.sharding import PartitionSpec as P

K = 256
DILATION_STEP = 12
H16 = 48
W16 = 72


def gelu_tanh(value):
    return jax.nn.gelu(value, approximate=True)


def padded_flat(flat_grid):
    reach = DILATION_STEP * W16 + DILATION_STEP
    return jnp.pad(flat_grid, ((0, 0), (reach, reach), (0, 0)))


def shifted(padded_grid, pixels, row_offset, column_offset):
    reach = DILATION_STEP * W16 + DILATION_STEP
    start = reach + DILATION_STEP * (row_offset * W16 + column_offset)
    view = padded_grid[:, start : start + pixels, :].astype(jnp.float32)
    column = jnp.arange(pixels, dtype=jnp.int32) % W16 + DILATION_STEP * column_offset
    keep = jnp.logical_and(column >= 0, column < W16)[:, None]
    return jnp.where(keep, view, 0.0)


def depthwise(flat_grid, kernel, sign):
    pixels = flat_grid.shape[1]
    padded_grid = padded_flat(flat_grid)
    total = jnp.zeros(flat_grid.shape, jnp.float32)
    for row_offset in range(-1, 2):
        for column_offset in range(-1, 2):
            index = 3 * (row_offset + 1) + (column_offset + 1)
            view = shifted(padded_grid, pixels, sign * row_offset, sign * column_offset)
            total = total + view * kernel[index].astype(jnp.float32)
    return total


def tap_sums(grad_mixed, flat_grid):
    pixels = flat_grid.shape[1]
    padded_grid = padded_flat(flat_grid)
    upstream = grad_mixed.astype(jnp.float32)
    rows_out = []
    for row_offset in range(-1, 2):
        for column_offset in range(-1, 2):
            view = shifted(padded_grid, pixels, row_offset, column_offset)
            rows_out.append(jnp.sum(upstream * view, axis=(0, 1)))
    return jnp.stack(rows_out, axis=0)


def on_device(features, depth_weight, point_weight, cotangent):
    samples, here, chans = features.shape
    parts = lax.axis_size("rows")
    slice_width = chans // parts
    blocks = jnp.transpose(features.reshape(samples, here, parts, slice_width), (2, 1, 0, 3))
    arrived = lax.all_to_all(blocks, "rows", split_axis=0, concat_axis=0, tiled=True)
    chan_field = jnp.transpose(arrived, (2, 0, 1, 3)).reshape(samples, parts * here, slice_width)
    chan_mixed = depthwise(chan_field, depth_weight, 1).astype(jnp.bfloat16)
    outgoing = jnp.transpose(chan_mixed.reshape(samples, parts, here, slice_width), (1, 2, 0, 3))
    returned = lax.all_to_all(outgoing, "rows", split_axis=0, concat_axis=0, tiled=True)
    row_mixed = jnp.transpose(returned, (2, 1, 0, 3)).reshape(samples * here, chans)
    pre = jnp.dot(row_mixed, point_weight, preferred_element_type=jnp.float32)
    act, pull = jax.vjp(gelu_tanh, pre)
    branch_out = act.astype(jnp.bfloat16).reshape(samples, here, K)
    grad_pre = pull(cotangent.reshape(-1, K).astype(jnp.float32))[0].astype(jnp.bfloat16)
    grad_pre_all = lax.all_gather(grad_pre.reshape(samples, here, K), "rows", axis=1, tiled=True)
    start = lax.axis_index("rows") * slice_width
    weight_own = lax.dynamic_slice_in_dim(point_weight, start, slice_width, axis=0)
    grad_chan = lax.dot_general(
        grad_pre_all, weight_own, (((2,), (1,)), ((), ())), preferred_element_type=jnp.float32
    ).astype(jnp.bfloat16)
    point_slice = lax.dot_general(
        chan_mixed, grad_pre_all, (((0, 1), (0, 1)), ((), ())), preferred_element_type=jnp.float32
    )
    grad_features = depthwise(grad_chan, depth_weight, -1).astype(jnp.bfloat16)
    depth_part = tap_sums(grad_chan, chan_field)
    taps = depth_part.shape[0]
    packed = jnp.concatenate(
        [point_slice, jnp.pad(depth_part, ((0, 0), (0, K - depth_part.shape[1])))], axis=0
    )
    summed = lax.all_gather(packed, "dp", axis=0, tiled=False).sum(axis=0)
    grad_point = summed[:slice_width]
    grad_depth = summed[slice_width : slice_width + taps, : depth_part.shape[1]]
    scale = 1.0 / math.sqrt(samples * lax.axis_size("dp") * H16 * W16)
    return (branch_out, grad_features, grad_point * scale, grad_depth * scale)


def solution(mesh):
    placed = (P("dp", "rows", None), P(None, "rows"), P(), P("dp", "rows", None))
    return jax.shard_map(
        on_device,
        mesh=mesh,
        in_specs=placed,
        out_specs=(P("dp", "rows", None), P("dp", None, "rows"), P("rows", None), P(None, "rows")),
        check_vma=False,
    )
```
